768 devices in a mesh: dp: 48 (over x, z_lo, core), tile: 16 (over z_hi, y).
Axes of the slice: x: 4, y: 8, z: 12 (z_hi: 2, z_lo: 6; z = z_hi * 6 + z_lo), core: 2. Of those that a mesh axis runs over, the one named last changes fastest.
Arguments:
- features: bfloat16 [48, 256, 128, 256], P('dp', 'tile'), may hold values from -6 to 6
- cotangent: bfloat16 [48, 256, 128, 256], P('dp', 'tile'), may hold values from -6 to 6
- conv_weight: bfloat16 [2304, 256], P('dp'), may hold values from -0.125 to 0.125
- norm_gain: float32 [256], replicated, may hold values from 0.1 to 1.9
- norm_bias: float32 [256], replicated, may hold values from -3 to 3
- film_rows: float32 [48, 512], P('dp'), may hold values from -3 to 3
Outputs:
- output: float32 [48, 256, 128, 256], P('dp', 'tile')
- grad_weight: float32 [2304, 256], P('dp', 'tile')
The draws below stay inside these ranges and needn't reach their ends.
All inputs are finite; a program needn't handle non-finite values.
Results may differ from the reference program's by a relative error of at most 0.0029.
Values may be sent and summed in bfloat16 or wider, within the bound.
No kernel may reach another device: no remote copies, remote signals or barrier semaphores. Data moves between devices by JAX's collectives and lax.ppermute only.
A program may use at most 64 MiB of HBM per device.

```python
import jax
import jax.numpy as jnp
from jax import lax

C = 256
G = 32
COLS = 128
SAMPLES = 48
HEIGHT = 256


def steps_of(own_key, dims, pieces, low, top_value):
    loudness = 1.0
    for position, parts in pieces:
        heights = jax.random.uniform(jax.random.fold_in(jax.random.fold_in(own_key, 6), position), (parts,), jnp.float32, low / len(pieces), top_value / len(pieces))
        loudness = loudness * jnp.repeat(jnp.exp(heights), dims[position] // parts).reshape((-1,) + (1,) * (len(dims) - 1 - position))
    return loudness


def normal_values(rng, shape, width, bound, split=(), dtype=jnp.bfloat16):
    entries = jax.random.normal(rng, shape, jnp.float32) * width
    if len(split) > 0:
        entries = steps_of(rng, shape, split, -0.22, 0.18) * entries
    return jnp.clip(entries, min=-bound, max=bound).astype(dtype)


def setup_inputs(seed: int = 0) -> dict:
    key_list = jax.random.split(jax.random.key(seed), 7)
    return {
        "features": normal_values(key_list[0], (SAMPLES, HEIGHT, COLS, C), 1.0, 6.0, ((0, 48), (1, 16))),
        "cotangent": normal_values(key_list[1], (SAMPLES, HEIGHT, COLS, C), 1.0, 6.0, ((0, 48), (1, 16))),
        "conv_weight": normal_values(key_list[2], (9 * C, C), (9 * C) ** -0.5, 0.125, ((0, 48),)),
        "norm_gain": jnp.clip(1.0 + 0.18 * jax.random.normal(key_list[3], (C,), jnp.float32), 0.1, 1.9),
        "norm_bias": normal_values(key_list[4], (C,), 0.5, 3.0, (), jnp.float32),
        "film_rows": normal_values(key_list[5], (SAMPLES, 2 * C), 0.5, 3.0, ((0, 48),), jnp.float32),
    }


def reference(features, cotangent, conv_weight, norm_gain, norm_bias, film_rows):
    kernel = conv_weight.reshape(3, 3, C, C)
    count = HEIGHT * COLS * (C // G)

    def one_sample(total, item):
        sample, cot, film = item
        values = sample.astype(jnp.float32)
        grouped = values.reshape(HEIGHT, COLS, G, C // G)
        mean = lax.optimization_barrier(jnp.sum(grouped, axis=(0, 1, 3))) / count
        var = lax.optimization_barrier(jnp.sum(grouped * grouped, axis=(0, 1, 3))) / count - mean * mean
        mean_c = jnp.repeat(mean, C // G)
        inv_c = jnp.repeat(1.0 / jnp.sqrt(var + 1e-05), C // G)
        normed = (values - mean_c) * inv_c * norm_gain + norm_bias
        act = jax.nn.silu(normed * (1.0 + film[:C]) + film[C:]).astype(jnp.bfloat16)
        conv = lax.conv_general_dilated(act[None], kernel, (1, 1), 'SAME', dimension_numbers=('NHWC', 'HWIO', 'NHWC'), preferred_element_type=jnp.float32)[0]
        result = conv + values
        padded = jnp.pad(act, ((1, 1), (1, 1), (0, 0)))
        taps = [padded[i:i + HEIGHT, j:j + COLS, :] for i in range(3) for j in range(3)]
        patches = jnp.concatenate(taps, axis=-1).reshape(HEIGHT * COLS, 9 * C)
        term = lax.dot_general(patches, cot.reshape(HEIGHT * COLS, C), (((0,), (0,)), ((), ())), preferred_element_type=jnp.float32)
        return (total + term, result)
    start = jnp.zeros((9 * C, C), jnp.float32)
    grad_sum, output = lax.scan(one_sample, start, (features, cotangent, film_rows))
    positions = SAMPLES * HEIGHT * COLS
    grad_weight = grad_sum / jnp.sqrt(jnp.float32(positions))
    return (output, grad_weight)
```

```python
import jax
import jax.numpy as jnp
from jax import lax
from jax.sharding import PartitionSpec as P

G = 32


def extended_2(cells, sides, width):
    for axis, dim in sides:
        count = lax.axis_size(axis)
        ends = count - 1
        head = lax.slice_in_dim(cells, 0, width, axis=dim)
        tail = lax.slice_in_dim(cells, cells.shape[dim] - width, cells.shape[dim], axis=dim)
        cells = jnp.concatenate(
            [
                lax.ppermute(tail, axis, [(i, (i + 1) % count) for i in range(ends)]),
                cells,
                lax.ppermute(head, axis, [((i + 1) % count, i) for i in range(ends)]),
            ],
            axis=dim,
        )
    return cells


def gather_a2a(x, axis):
    n = lax.axis_size(axis)
    spread = jnp.broadcast_to(x[None], (n,) + x.shape)
    got = lax.all_to_all(spread, axis, 0, 0)
    return got.reshape((n * x.shape[0],) + x.shape[1:])


def sum_a2a(x, axis):
    got = lax.all_to_all(x, axis, 0, 0)
    return jnp.sum(got, axis=0)


def body(features, cotangent, conv_weight, norm_gain, norm_bias, film_rows):
    rows = features.shape[1]
    cols = features.shape[2]
    width = features.shape[3]
    ndp = lax.axis_size("dp")
    ntile = lax.axis_size("tile")
    full_weight = gather_a2a(conv_weight, "dp")
    values = features[0].astype(jnp.float32)
    grouped = values.reshape(rows, cols, G, width // G)
    stats = jnp.concatenate([jnp.sum(grouped, axis=(0, 1, 3)), jnp.sum(grouped * grouped, axis=(0, 1, 3))])
    stats = sum_a2a(jnp.broadcast_to(stats[None], (ntile,) + stats.shape), "tile")
    sums, squares = stats[:G], stats[G:]
    count = rows * ntile * cols * (width // G)
    mean = sums / count
    var = squares / count - mean * mean
    mean_c = jnp.repeat(mean, width // G)
    inv_c = jnp.repeat(1.0 / jnp.sqrt(var + 1e-05), width // G)
    film = film_rows[0]
    normed = (values - mean_c) * inv_c * norm_gain + norm_bias
    act = jax.nn.silu(normed * (1.0 + film[:width]) + film[width:]).astype(jnp.bfloat16)
    extended = extended_2(act, (("tile", 0),), 1)
    padded = jnp.pad(extended, ((0, 0), (1, 1), (0, 0)))
    taps = [padded[i : i + rows, j : j + cols, :] for i in range(3) for j in range(3)]
    patches = jnp.concatenate(taps, axis=-1).reshape(rows * cols, 9 * width)
    positions = ndp * rows * ntile * cols
    cot_rows = cotangent[0].reshape(rows * cols, width)
    partial = lax.dot_general(
        patches, cot_rows, (((0,), (0,)), ((), ())), preferred_element_type=jnp.float32
    )
    kdim = partial.shape[0]
    summed_rows = sum_a2a(partial.reshape(ndp, kdim // ndp, width), "dp")
    blocks = summed_rows.reshape(kdim // ndp, ntile, width // ntile).transpose(1, 0, 2)
    grad_sum = sum_a2a(blocks, "tile")
    grad_weight = grad_sum / jnp.sqrt(jnp.float32(positions))
    conv = jnp.dot(patches, full_weight, preferred_element_type=jnp.float32)
    output = (conv.reshape(rows, cols, width) + values)[None]
    return (output, grad_weight)


def solution(mesh):
    in_specs = (
        P("dp", "tile", None, None),
        P("dp", "tile", None, None),
        P("dp", None),
        P(),
        P(),
        P("dp", None),
    )
    out_specs = (P("dp", "tile", None, None), P("dp", "tile"))
    return jax.shard_map(body, mesh=mesh, in_specs=in_specs, out_specs=out_specs, check_vma=False)
```

```python
import jax
import jax.numpy as jnp
from jax import lax
from jax.sharding import PartitionSpec as P

G = 32

DP_SUB = {"x": (12, 4), "zl": (2, 6), "c": (1, 2)}
TILE_SUB = {"zh": (8, 2), "y": (1, 8)}


def sub_of(name):
    if name in DP_SUB:
        return ("dp",) + DP_SUB[name]
    return ("tile",) + TILE_SUB[name]


def shift_pairs(total, stride, size, j):
    pairs = []
    for i in range(total):
        k = (i // stride) % size
        pairs.append((i, i + ((k + j) % size - k) * stride))
    return pairs


def coord(axis, stride, size):
    return (lax.axis_index(axis) // stride) % size


def extended_2(cells, sides, width):
    for axis, dim in sides:
        count = lax.axis_size(axis)
        ends = count - 1
        head = lax.slice_in_dim(cells, 0, width, axis=dim)
        tail = lax.slice_in_dim(cells, cells.shape[dim] - width, cells.shape[dim], axis=dim)
        cells = jnp.concatenate(
            [
                lax.ppermute(tail, axis, [(i, (i + 1) % count) for i in range(ends)]),
                cells,
                lax.ppermute(head, axis, [((i + 1) % count, i) for i in range(ends)]),
            ],
            axis=dim,
        )
    return cells


def stage_gather(y, name):
    axis, stride, size = sub_of(name)
    total = lax.axis_size(axis)
    k = coord(axis, stride, size)
    out = jnp.zeros((size,) + y.shape, y.dtype)
    out = lax.dynamic_update_index_in_dim(out, y, k, 0)
    for j in range(1, size):
        got = lax.ppermute(y, axis, shift_pairs(total, stride, size, j))
        out = lax.dynamic_update_index_in_dim(out, got, (k - j) % size, 0)
    return out


def stage_scatter(x, name):
    axis, stride, size = sub_of(name)
    total = lax.axis_size(axis)
    k = coord(axis, stride, size)
    acc = lax.dynamic_index_in_dim(x, k, 0, keepdims=False)
    for j in range(1, size):
        piece = lax.dynamic_index_in_dim(x, (k + j) % size, 0, keepdims=False)
        acc = acc + lax.ppermute(piece, axis, shift_pairs(total, stride, size, j))
    return acc


def tile_allreduce(v):
    total = lax.axis_size("tile")
    step = 1
    while step < total:
        v = v + lax.ppermute(v, "tile", [(i, i ^ step) for i in range(total)])
        step *= 2
    return v


def body(features, cotangent, conv_weight, norm_gain, norm_bias, film_rows):
    rows = features.shape[1]
    cols = features.shape[2]
    width = features.shape[3]
    ndp = lax.axis_size("dp")
    ntile = lax.axis_size("tile")
    w = stage_gather(conv_weight, "c")
    w = stage_gather(w, "zl")
    w = stage_gather(w, "x")
    full_weight = w.reshape(ndp * conv_weight.shape[0], width)
    values = features[0].astype(jnp.float32)
    grouped = values.reshape(rows, cols, G, width // G)
    stats = jnp.concatenate([jnp.sum(grouped, axis=(0, 1, 3)), jnp.sum(grouped * grouped, axis=(0, 1, 3))])
    stats = tile_allreduce(stats)
    sums, squares = stats[:G], stats[G:]
    count = rows * ntile * cols * (width // G)
    mean = sums / count
    var = squares / count - mean * mean
    mean_c = jnp.repeat(mean, width // G)
    inv_c = jnp.repeat(1.0 / jnp.sqrt(var + 1e-05), width // G)
    film = film_rows[0]
    normed = (values - mean_c) * inv_c * norm_gain + norm_bias
    act = jax.nn.silu(normed * (1.0 + film[:width]) + film[width:]).astype(jnp.bfloat16)
    extended = extended_2(act, (("tile", 0),), 1)
    padded = jnp.pad(extended, ((0, 0), (1, 1), (0, 0)))
    taps = [padded[i : i + rows, j : j + cols, :] for i in range(3) for j in range(3)]
    patches = jnp.concatenate(taps, axis=-1).reshape(rows * cols, 9 * width)
    positions = ndp * rows * ntile * cols
    cot_rows = cotangent[0].reshape(rows * cols, width)
    part_t = lax.dot_general(
        cot_rows, patches, (((0,), (0,)), ((), ())), preferred_element_type=jnp.float32
    )
    kdim = part_t.shape[1]
    per = kdim // ndp
    q = width // ntile
    g = part_t.reshape(2, 8, q, 4, 6, 2, per)
    g = g.transpose(5, 1, 4, 3, 0, 6, 2).reshape(2, 8, 6, 4, 2, per * q)
    g = stage_scatter(g, "c")
    g = stage_scatter(g, "y")
    g = stage_scatter(g, "zl")
    g = stage_scatter(g, "x")
    g = stage_scatter(g, "zh")
    grad_weight = g.reshape(per, q) / jnp.sqrt(jnp.float32(positions))
    conv = jnp.dot(patches, full_weight, preferred_element_type=jnp.float32)
    output = (conv.reshape(rows, cols, width) + values)[None]
    return (output, grad_weight)


def solution(mesh):
    in_specs = (
        P("dp", "tile", None, None),
        P("dp", "tile", None, None),
        P("dp", None),
        P(),
        P(),
        P("dp", None),
    )
    out_specs = (P("dp", "tile", None, None), P("dp", "tile"))
    return jax.shard_map(body, mesh=mesh, in_specs=in_specs, out_specs=out_specs, check_vma=False)
```

```python
import jax
import jax.numpy as jnp
from jax import lax
from jax.sharding import PartitionSpec as P

G = 32


def coord(axis, stride, size):
    return (lax.axis_index(axis) // stride) % size


def halve(x, dim, axis, stride):
    total = lax.axis_size(axis)
    k = coord(axis, stride, 2)
    pairs = [(i, i + (1 - 2 * ((i // stride) % 2)) * stride) for i in range(total)]
    mine = lax.dynamic_index_in_dim(x, k, dim, keepdims=False)
    other = lax.dynamic_index_in_dim(x, 1 - k, dim, keepdims=False)
    return mine + lax.ppermute(other, axis, pairs)


def direct(x, dim, axis, stride, size):
    total = lax.axis_size(axis)
    k = coord(axis, stride, size)
    acc = lax.dynamic_index_in_dim(x, k, dim, keepdims=False)
    for j in range(1, size):
        pairs = []
        for i in range(total):
            m = (i // stride) % size
            pairs.append((i, i + ((m + j) % size - m) * stride))
        piece = lax.dynamic_index_in_dim(x, (k + j) % size, dim, keepdims=False)
        acc = acc + lax.ppermute(piece, axis, pairs)
    return acc


def gather_a2a(x, axis):
    n = lax.axis_size(axis)
    spread = jnp.broadcast_to(x[None], (n,) + x.shape)
    got = lax.all_to_all(spread, axis, 0, 0)
    return got.reshape((n * x.shape[0],) + x.shape[1:])


def body(features, cotangent, conv_weight, norm_gain, norm_bias, film_rows):
    rows = features.shape[1]
    cols = features.shape[2]
    width = features.shape[3]
    ndp = lax.axis_size("dp")
    ntile = lax.axis_size("tile")
    t = lax.axis_index("tile")
    full_weight = gather_a2a(conv_weight, "dp")
    raw = features[0]
    above = lax.ppermute(raw[rows - 1 :], "tile", [(i, i + 1) for i in range(ntile - 1)])
    below = lax.ppermute(raw[:1], "tile", [(i + 1, i) for i in range(ntile - 1)])
    values = raw.astype(jnp.float32)
    grouped = values.reshape(rows, cols, G, width // G)
    stats = jnp.concatenate([jnp.sum(grouped, axis=(0, 1, 3)), jnp.sum(grouped * grouped, axis=(0, 1, 3))])
    stats = jnp.sum(lax.all_to_all(jnp.broadcast_to(stats[None], (ntile,) + stats.shape), "tile", 0, 0), axis=0)
    sums, squares = stats[:G], stats[G:]
    count = rows * ntile * cols * (width // G)
    mean = sums / count
    var = squares / count - mean * mean
    mean_c = jnp.repeat(mean, width // G)
    inv_c = jnp.repeat(1.0 / jnp.sqrt(var + 1e-05), width // G)
    film = film_rows[0]
    ext = jnp.concatenate([above, raw, below], axis=0).astype(jnp.float32)
    normed = (ext - mean_c) * inv_c * norm_gain + norm_bias
    act = jax.nn.silu(normed * (1.0 + film[:width]) + film[width:]).astype(jnp.bfloat16)
    row_id = lax.broadcasted_iota(jnp.int32, (rows + 2, 1, 1), 0)
    outside = ((row_id == 0) & (t == 0)) | ((row_id == rows + 1) & (t == ntile - 1))
    act = jnp.where(outside, jnp.zeros_like(act), act)
    padded = jnp.pad(act, ((0, 0), (1, 1), (0, 0)))
    taps = [padded[i : i + rows, j : j + cols, :] for i in range(3) for j in range(3)]
    patches = jnp.concatenate(taps, axis=-1).reshape(rows * cols, 9 * width)
    positions = ndp * rows * ntile * cols
    cot_rows = cotangent[0].reshape(rows * cols, width)
    part_t = lax.dot_general(
        cot_rows, patches, (((0,), (0,)), ((), ())), preferred_element_type=jnp.float32
    )
    per = part_t.shape[1] // ndp
    q = width // ntile
    g = part_t.T.reshape(2, 2, 3, 2, 2, per, width)
    g = halve(g, 4, "dp", 1)
    g = halve(g, 0, "dp", 24)
    g = halve(g, 0, "dp", 12)
    g = direct(g, 0, "dp", 4, 3)
    g = halve(g, 0, "dp", 2)
    span = width
    for stride in (8, 4, 2, 1):
        span //= 2
        g = halve(g.reshape(per, 2, span), 1, "tile", stride)
    grad_weight = g / jnp.sqrt(jnp.float32(positions))
    conv = jnp.dot(patches, full_weight, preferred_element_type=jnp.float32)
    output = (conv.reshape(rows, cols, width) + values)[None]
    return (output, grad_weight)


def solution(mesh):
    in_specs = (
        P("dp", "tile", None, None),
        P("dp", "tile", None, None),
        P("dp", None),
        P(),
        P(),
        P("dp", None),
    )
    out_specs = (P("dp", "tile", None, None), P("dp", "tile"))
    return jax.shard_map(body, mesh=mesh, in_specs=in_specs, out_specs=out_specs, check_vma=False)
```

```python
import jax
import jax.numpy as jnp
from jax import lax
from jax.sharding import PartitionSpec as P

G = 32


def coord(axis, stride, size):
    return (lax.axis_index(axis) // stride) % size


def halve(x, dim, axis, stride):
    total = lax.axis_size(axis)
    k = coord(axis, stride, 2)
    pairs = [(i, i + (1 - 2 * ((i // stride) % 2)) * stride) for i in range(total)]
    mine = lax.dynamic_index_in_dim(x, k, dim, keepdims=False)
    other = lax.dynamic_index_in_dim(x, 1 - k, dim, keepdims=False)
    return mine + lax.ppermute(other, axis, pairs)


def direct(x, dim, axis, stride, size):
    total = lax.axis_size(axis)
    k = coord(axis, stride, size)
    acc = lax.dynamic_index_in_dim(x, k, dim, keepdims=False)
    for j in range(1, size):
        pairs = []
        for i in range(total):
            m = (i // stride) % size
            pairs.append((i, i + ((m + j) % size - m) * stride))
        piece = lax.dynamic_index_in_dim(x, (k + j) % size, dim, keepdims=False)
        acc = acc + lax.ppermute(piece, axis, pairs)
    return acc


def gather_a2a(x, axis):
    n = lax.axis_size(axis)
    spread = jnp.broadcast_to(x[None], (n,) + x.shape)
    got = lax.all_to_all(spread, axis, 0, 0)
    return got.reshape((n * x.shape[0],) + x.shape[1:])


def body(features, cotangent, conv_weight, norm_gain, norm_bias, film_rows):
    rows = features.shape[1]
    cols = features.shape[2]
    width = features.shape[3]
    ndp = lax.axis_size("dp")
    ntile = lax.axis_size("tile")
    t = lax.axis_index("tile")
    full_weight = lax.all_gather(conv_weight, "dp", axis=0, tiled=True)
    raw = features[0]
    above = lax.ppermute(raw[rows - 1 :], "tile", [(i, i + 1) for i in range(ntile - 1)])
    below = lax.ppermute(raw[:1], "tile", [(i + 1, i) for i in range(ntile - 1)])
    values = raw.astype(jnp.float32)
    grouped = values.reshape(rows, cols, G, width // G)
    stats = jnp.concatenate([jnp.sum(grouped, axis=(0, 1, 3)), jnp.sum(grouped * grouped, axis=(0, 1, 3))])
    stats = jnp.sum(lax.all_to_all(jnp.broadcast_to(stats[None], (ntile,) + stats.shape), "tile", 0, 0), axis=0)
    sums, squares = stats[:G], stats[G:]
    count = rows * ntile * cols * (width // G)
    mean = sums / count
    var = squares / count - mean * mean
    mean_c = jnp.repeat(mean, width // G)
    inv_c = jnp.repeat(1.0 / jnp.sqrt(var + 1e-05), width // G)
    film = film_rows[0]
    ext = jnp.concatenate([above, raw, below], axis=0).astype(jnp.float32)
    normed = (ext - mean_c) * inv_c * norm_gain + norm_bias
    act = jax.nn.silu(normed * (1.0 + film[:width]) + film[width:]).astype(jnp.bfloat16)
    row_id = lax.broadcasted_iota(jnp.int32, (rows + 2, 1, 1), 0)
    outside = ((row_id == 0) & (t == 0)) | ((row_id == rows + 1) & (t == ntile - 1))
    act = jnp.where(outside, jnp.zeros_like(act), act)
    padded = jnp.pad(act, ((0, 0), (1, 1), (0, 0)))
    taps = [padded[i : i + rows, j : j + cols, :] for i in range(3) for j in range(3)]
    patches = jnp.concatenate(taps, axis=-1).reshape(rows * cols, 9 * width)
    positions = ndp * rows * ntile * cols
    cot_rows = cotangent[0].reshape(rows * cols, width)
    part_t = lax.optimization_barrier(
        lax.dot_general(cot_rows, patches, (((0,), (0,)), ((), ())), preferred_element_type=jnp.float32)
    )
    per = part_t.shape[1] // ndp
    q = width // ntile
    g = part_t.T.reshape(2, 2, 3, 2, 2, per, width)
    g = halve(g, 4, "dp", 1)
    g = halve(g, 0, "dp", 24)
    g = halve(g, 0, "dp", 12)
    g = direct(g, 0, "dp", 4, 3)
    g = halve(g, 0, "dp", 2)
    span = width
    for stride in (8, 4, 2, 1):
        span //= 2
        g = halve(g.reshape(per, 2, span), 1, "tile", stride)
    grad_weight = g / jnp.sqrt(jnp.float32(positions))
    conv = jnp.dot(patches, full_weight, preferred_element_type=jnp.float32)
    output = (conv.reshape(rows, cols, width) + values)[None]
    return (output, grad_weight)


def solution(mesh):
    in_specs = (
        P("dp", "tile", None, None),
        P("dp", "tile", None, None),
        P("dp", None),
        P(),
        P(),
        P("dp", None),
    )
    out_specs = (P("dp", "tile", None, None), P("dp", "tile"))
    return jax.shard_map(body, mesh=mesh, in_specs=in_specs, out_specs=out_specs, check_vma=False)
```

```python
import jax
import jax.numpy as jnp
from jax import lax
from jax.sharding import PartitionSpec as P

G = 32


def coord(axis, stride, size):
    return (lax.axis_index(axis) // stride) % size


def halve(x, dim, axis, stride):
    total = lax.axis_size(axis)
    k = coord(axis, stride, 2)
    pairs = [(i, i + (1 - 2 * ((i // stride) % 2)) * stride) for i in range(total)]
    mine = lax.dynamic_index_in_dim(x, k, dim, keepdims=False)
    other = lax.dynamic_index_in_dim(x, 1 - k, dim, keepdims=False)
    return mine + lax.ppermute(other, axis, pairs)


def direct(x, dim, axis, stride, size):
    total = lax.axis_size(axis)
    k = coord(axis, stride, size)
    acc = lax.dynamic_index_in_dim(x, k, dim, keepdims=False)
    for j in range(1, size):
        pairs = []
        for i in range(total):
            m = (i // stride) % size
            pairs.append((i, i + ((m + j) % size - m) * stride))
        piece = lax.dynamic_index_in_dim(x, (k + j) % size, dim, keepdims=False)
        acc = acc + lax.ppermute(piece, axis, pairs)
    return acc


def body_inner(features, cotangent, conv_weight, norm_gain, norm_bias, film_rows):
    rows = features.shape[1]
    cols = features.shape[2]
    width = features.shape[3]
    ndp = lax.axis_size("dp")
    ntile = lax.axis_size("tile")
    t = lax.axis_index("tile")
    full_weight = lax.all_gather(conv_weight, "dp", axis=0, tiled=True)
    raw = features[0]
    above = lax.ppermute(raw[rows - 1 :], "tile", [(i, i + 1) for i in range(ntile - 1)])
    below = lax.ppermute(raw[:1], "tile", [(i + 1, i) for i in range(ntile - 1)])
    values = raw.astype(jnp.float32)
    grouped = values.reshape(rows, cols, G, width // G)
    stats = jnp.concatenate([jnp.sum(grouped, axis=(0, 1, 3)), jnp.sum(grouped * grouped, axis=(0, 1, 3))])
    stats = jnp.sum(lax.all_to_all(jnp.broadcast_to(stats[None], (ntile,) + stats.shape), "tile", 0, 0), axis=0)
    sums, squares = stats[:G], stats[G:]
    count = rows * ntile * cols * (width // G)
    mean = sums / count
    var = squares / count - mean * mean
    mean_c = jnp.repeat(mean, width // G)
    inv_c = jnp.repeat(1.0 / jnp.sqrt(var + 1e-05), width // G)
    film = film_rows[0]
    ext = jnp.concatenate([above, raw, below], axis=0).astype(jnp.float32)
    normed = (ext - mean_c) * inv_c * norm_gain + norm_bias
    act = jax.nn.silu(normed * (1.0 + film[:width]) + film[width:]).astype(jnp.bfloat16)
    row_id = lax.broadcasted_iota(jnp.int32, (rows + 2, 1, 1), 0)
    outside = ((row_id == 0) & (t == 0)) | ((row_id == rows + 1) & (t == ntile - 1))
    act = jnp.where(outside, jnp.zeros_like(act), act)
    padded = jnp.pad(act, ((0, 0), (1, 1), (0, 0)))
    taps = [padded[i : i + rows, j : j + cols, :] for i in range(3) for j in range(3)]
    patches = jnp.concatenate(taps, axis=-1).reshape(rows * cols, 9 * width)
    positions = ndp * rows * ntile * cols
    cot_rows = cotangent[0].reshape(rows * cols, width)
    part_t = lax.optimization_barrier(
        lax.dot_general(cot_rows, patches, (((0,), (0,)), ((), ())), preferred_element_type=jnp.float32)
    )
    per = part_t.shape[1] // ndp
    g = part_t.T.reshape(2, 2, 3, 2, 2, per, width)
    g = halve(g, 4, "dp", 1)
    g = halve(g, 1, "dp", 12)
    g = halve(g, 0, "dp", 24)
    g = direct(g, 0, "dp", 4, 3)
    g = halve(g, 0, "dp", 2)
    span = width
    for stride in (8, 4, 2, 1):
        span //= 2
        g = halve(g.reshape(per, 2, span), 1, "tile", stride)
    grad_weight = g / jnp.sqrt(jnp.float32(positions))
    conv = jnp.dot(patches, full_weight, preferred_element_type=jnp.float32)
    output = (conv.reshape(rows, cols, width) + values)[None]
    return (output, grad_weight)


def solution(mesh):
    in_specs = (
        P("dp", "tile", None, None),
        P("dp", "tile", None, None),
        P("dp", None),
        P(),
        P(),
        P("dp", None),
    )
    out_specs = (P("dp", "tile", None, None), P("dp", "tile"))
    return jax.shard_map(body_inner, mesh=mesh, in_specs=in_specs, out_specs=out_specs, check_vma=False)
```

```python
import jax
import jax.numpy as jnp
from jax import lax
from jax.sharding import PartitionSpec as P

G = 32


def coord(axis, stride, size):
    return (lax.axis_index(axis) // stride) % size


def halve(x, dim, axis, stride):
    total = lax.axis_size(axis)
    k = coord(axis, stride, 2)
    pairs = [(i, i + (1 - 2 * ((i // stride) % 2)) * stride) for i in range(total)]
    mine = lax.dynamic_index_in_dim(x, k, dim, keepdims=False)
    other = lax.dynamic_index_in_dim(x, 1 - k, dim, keepdims=False)
    return mine + lax.ppermute(other, axis, pairs)


def direct(x, dim, axis, stride, size):
    total = lax.axis_size(axis)
    k = coord(axis, stride, size)
    acc = lax.dynamic_index_in_dim(x, k, dim, keepdims=False)
    for j in range(1, size):
        pairs = []
        for i in range(total):
            m = (i // stride) % size
            pairs.append((i, i + ((m + j) % size - m) * stride))
        piece = lax.dynamic_index_in_dim(x, (k + j) % size, dim, keepdims=False)
        acc = acc + lax.ppermute(piece, axis, pairs)
    return acc


def body_inner(features, cotangent, conv_weight, norm_gain, norm_bias, film_rows):
    rows = features.shape[1]
    cols = features.shape[2]
    width = features.shape[3]
    ndp = lax.axis_size("dp")
    ntile = lax.axis_size("tile")
    t = lax.axis_index("tile")
    full_weight = lax.all_gather(conv_weight, "dp", axis=0, tiled=True)
    raw = features[0]
    above = lax.ppermute(raw[rows - 1 :], "tile", [(i, i + 1) for i in range(ntile - 1)])
    below = lax.ppermute(raw[:1], "tile", [(i + 1, i) for i in range(ntile - 1)])
    values = raw.astype(jnp.float32)
    grouped = values.reshape(rows, cols, G, width // G)
    stats = jnp.concatenate([jnp.sum(grouped, axis=(0, 1, 3)), jnp.sum(grouped * grouped, axis=(0, 1, 3))])
    stats = lax.all_to_all(jnp.broadcast_to(stats[None], (ntile,) + stats.shape), "tile", 0, 0)
    stats = jnp.sum(stats, axis=0)
    sums, squares = stats[:G], stats[G:]
    count = rows * ntile * cols * (width // G)
    mean = sums / count
    var = squares / count - mean * mean
    mean_c = jnp.repeat(mean, width // G)
    inv_c = jnp.repeat(1.0 / jnp.sqrt(var + 1e-05), width // G)
    film = film_rows[0]
    ext = jnp.concatenate([above, raw, below], axis=0).astype(jnp.float32)
    normed = (ext - mean_c) * inv_c * norm_gain + norm_bias
    act = jax.nn.silu(normed * (1.0 + film[:width]) + film[width:]).astype(jnp.bfloat16)
    row_id = lax.broadcasted_iota(jnp.int32, (rows + 2, 1, 1), 0)
    outside = ((row_id == 0) & (t == 0)) | ((row_id == rows + 1) & (t == ntile - 1))
    act = jnp.where(outside, jnp.zeros_like(act), act)
    padded = jnp.pad(act, ((0, 0), (1, 1), (0, 0)))
    taps = [padded[i : i + rows, j : j + cols, :] for i in range(3) for j in range(3)]
    patches = jnp.concatenate(taps, axis=-1).reshape(rows * cols, 9 * width)
    positions = ndp * rows * ntile * cols
    cot_rows = cotangent[0].reshape(rows * cols, width)
    part_t = lax.optimization_barrier(
        lax.dot_general(cot_rows, patches, (((0,), (0,)), ((), ())), preferred_element_type=jnp.float32)
    )
    per = part_t.shape[1] // ndp
    g = part_t.T.reshape(2, 2, 3, 2, 2, per, width)
    g = halve(g, 4, "dp", 1)
    half = width // 2
    ga = halve(g[..., :half], 1, "dp", 12)
    gb = halve(g[..., half:], 3, "dp", 2)
    ga = halve(ga, 2, "dp", 2)
    gb = halve(gb, 1, "dp", 12)
    g = jnp.concatenate([ga, gb], axis=-1)
    g = halve(g, 0, "dp", 24)
    g = direct(g, 0, "dp", 4, 3)
    span = width
    for stride in (8, 4, 2, 1):
        span //= 2
        g = halve(g.reshape(per, 2, span), 1, "tile", stride)
    grad_weight = g / jnp.sqrt(jnp.float32(positions))
    conv = jnp.dot(patches, full_weight, preferred_element_type=jnp.float32)
    output = (conv.reshape(rows, cols, width) + values)[None]
    return (output, grad_weight)


def solution(mesh):
    in_specs = (
        P("dp", "tile", None, None),
        P("dp", "tile", None, None),
        P("dp", None),
        P(),
        P(),
        P("dp", None),
    )
    out_specs = (P("dp", "tile", None, None), P("dp", "tile"))
    return jax.shard_map(body_inner, mesh=mesh, in_specs=in_specs, out_specs=out_specs, check_vma=False)
```

```python
import jax
import jax.numpy as jnp
from jax import lax
from jax.sharding import PartitionSpec as P

G = 32


def coord(axis, stride, size):
    return (lax.axis_index(axis) // stride) % size


def halve(x, dim, axis, stride):
    total = lax.axis_size(axis)
    k = coord(axis, stride, 2)
    pairs = [(i, i + (1 - 2 * ((i // stride) % 2)) * stride) for i in range(total)]
    mine = lax.dynamic_index_in_dim(x, k, dim, keepdims=False)
    other = lax.dynamic_index_in_dim(x, 1 - k, dim, keepdims=False)
    return mine + lax.ppermute(other, axis, pairs)


def direct(x, dim, axis, stride, size):
    total = lax.axis_size(axis)
    k = coord(axis, stride, size)
    acc = lax.dynamic_index_in_dim(x, k, dim, keepdims=False)
    for j in range(1, size):
        pairs = []
        for i in range(total):
            m = (i // stride) % size
            pairs.append((i, i + ((m + j) % size - m) * stride))
        piece = lax.dynamic_index_in_dim(x, (k + j) % size, dim, keepdims=False)
        acc = acc + lax.ppermute(piece, axis, pairs)
    return acc


def body_inner(features, cotangent, conv_weight, norm_gain, norm_bias, film_rows):
    rows = features.shape[1]
    cols = features.shape[2]
    width = features.shape[3]
    ndp = lax.axis_size("dp")
    ntile = lax.axis_size("tile")
    t = lax.axis_index("tile")
    full_weight = lax.all_gather(conv_weight, "dp", axis=0, tiled=True)
    raw = features[0]
    above = lax.ppermute(raw[rows - 1 :], "tile", [(i, i + 1) for i in range(ntile - 1)])
    below = lax.ppermute(raw[:1], "tile", [(i + 1, i) for i in range(ntile - 1)])
    values = raw.astype(jnp.float32)
    grouped = values.reshape(rows, cols, G, width // G)
    stats = jnp.concatenate([jnp.sum(grouped, axis=(0, 1, 3)), jnp.sum(grouped * grouped, axis=(0, 1, 3))])
    stats = jnp.sum(lax.all_to_all(jnp.broadcast_to(stats[None], (ntile,) + stats.shape), "tile", 0, 0), axis=0)
    sums, squares = stats[:G], stats[G:]
    count = rows * ntile * cols * (width // G)
    mean = sums / count
    var = squares / count - mean * mean
    mean_c = jnp.repeat(mean, width // G)
    inv_c = jnp.repeat(1.0 / jnp.sqrt(var + 1e-05), width // G)
    film = film_rows[0]
    ext = jnp.concatenate([above, raw, below], axis=0).astype(jnp.float32)
    normed = (ext - mean_c) * inv_c * norm_gain + norm_bias
    act = jax.nn.silu(normed * (1.0 + film[:width]) + film[width:]).astype(jnp.bfloat16)
    row_id = lax.broadcasted_iota(jnp.int32, (rows + 2, 1, 1), 0)
    outside = ((row_id == 0) & (t == 0)) | ((row_id == rows + 1) & (t == ntile - 1))
    act = jnp.where(outside, jnp.zeros_like(act), act)
    padded = jnp.pad(act, ((0, 0), (1, 1), (0, 0)))
    taps = [padded[i : i + rows, j : j + cols, :] for i in range(3) for j in range(3)]
    patches = jnp.concatenate(taps, axis=-1).reshape(rows * cols, 9 * width)
    positions = ndp * rows * ntile * cols
    cot_rows = cotangent[0].reshape(rows * cols, width)
    part_t = lax.optimization_barrier(
        lax.dot_general(cot_rows, patches, (((0,), (0,)), ((), ())), preferred_element_type=jnp.float32)
    )
    per = part_t.shape[1] // ndp
    g = part_t.T.reshape(2, 2, 3, 2, 2, per, width)
    g = halve(g, 4, "dp", 1)
    half = width // 2
    ga = halve(g[..., :half], 1, "dp", 12)
    gb = halve(g[..., half:], 3, "dp", 2)
    ga = halve(ga, 2, "dp", 2)
    gb = halve(gb, 1, "dp", 12)
    g = jnp.concatenate([ga, gb], axis=-1)
    quarter = half // 2
    ga = halve(g[..., :half], 0, "dp", 24)
    gb = halve(g[..., half:].reshape(g.shape[:-1] + (2, quarter)), 3, "tile", 4)
    ga = halve(ga.reshape(ga.shape[:-1] + (2, quarter)), 2, "tile", 4)
    gb = halve(gb, 0, "dp", 24)
    g = jnp.stack([ga, gb], axis=2)
    g = direct(g, 0, "dp", 4, 3)
    g = halve(g, 1, "tile", 8)
    span = quarter
    for stride in (2, 1):
        span //= 2
        g = halve(g.reshape(per, 2, span), 1, "tile", stride)
    grad_weight = g / jnp.sqrt(jnp.float32(positions))
    conv = jnp.dot(patches, full_weight, preferred_element_type=jnp.float32)
    output = (conv.reshape(rows, cols, width) + values)[None]
    return (output, grad_weight)


def solution(mesh):
    in_specs = (
        P("dp", "tile", None, None),
        P("dp", "tile", None, None),
        P("dp", None),
        P(),
        P(),
        P("dp", None),
    )
    out_specs = (P("dp", "tile", None, None), P("dp", "tile"))
    return jax.shard_map(body_inner, mesh=mesh, in_specs=in_specs, out_specs=out_specs, check_vma=False)
```
